128 devices in a mesh: group: 4 (over y_lo, core), fsdp: 32 (over y_hi, x, z).
Axes of the slice: x: 4, y: 4 (y_hi: 2, y_lo: 2; y = y_hi * 2 + y_lo), z: 4, core: 2. Of those that a mesh axis runs over, the one named last changes fastest.
Arguments:
- anchor: bfloat16 [8192, 1024], P('fsdp'), may hold values from -6 to 6
- pseudo_grads: bfloat16 [4, 8192, 1024], P('group', 'fsdp'), may hold values from -1.5 to 1.5
- outer_moment: float32 [8192, 1024], P('fsdp'), may hold values from -1.2 to 1.2
- adam_first: float32 [4, 8192, 1024], P('group', 'fsdp'), may hold values from -1.8 to 1.8
- adam_second: float32 [4, 8192, 1024], P('group', 'fsdp'), may hold values from 0.25 to 4
- inputs: bfloat16 [32768, 8192], P(('group', 'fsdp')), may hold values from -24 to 24
- key_cotangent: bfloat16 [32768, 1024], P(('group', 'fsdp')), may hold values from -6 to 6
Outputs:
- new_anchor: bfloat16 [8192, 1024], P('fsdp')
- new_moment: float32 [8192, 1024], P('fsdp')
- inner_weights: bfloat16 [4, 8192, 1024], P('group', 'fsdp')
- first_moment: float32 [4, 8192, 1024], P('group', 'fsdp')
- second_moment: float32 [4, 8192, 1024], P('group', 'fsdp')
- input_grad: bfloat16 [32768, 8192], P(('group', 'fsdp'))
The draws below stay inside these ranges and needn't reach their ends.
All inputs are finite; a program needn't handle non-finite values.
Results may differ from the reference program's by a relative error of at most 0.012.
Values may be sent and summed in bfloat16 or wider, within the bound.
No kernel may reach another device: no remote copies, remote signals or barrier semaphores. Data moves between devices by JAX's collectives and lax.ppermute only.
A program may use at most 128 MiB of HBM per device.

```python
import math
import jax
import jax.numpy as jnp
from jax import lax

D = 8192
KV = 1024
TOK_DEV = 256
GROUPS = 4
TOKENS = 32768
N_GROUP = 4
N_FSDP = 32


def spiked(entries, key, source, target, parts, factor):
    def block_of(position):
        return (jnp.arange(entries.shape[position]) // (entries.shape[position] // parts)).reshape((-1,) + (1,) * (entries.ndim - 1 - position))

    one_side = jax.random.permutation(key, parts)[block_of(target)]
    other_side = (block_of(target) + parts // 2) % parts
    return jnp.where((block_of(source) == one_side) | (block_of(source) == other_side), factor * entries, entries)


def shard_levels(key, shape, shards, low, top_value):
    loudness = 1.0
    for axis_at, parts in shards:
        steps = jax.random.uniform(jax.random.fold_in(jax.random.fold_in(key, 6), axis_at), (parts,), jnp.float32, low / len(shards), top_value / len(shards))
        loudness = loudness * jnp.repeat(jnp.exp(steps), shape[axis_at] // parts).reshape((-1,) + (1,) * (len(shape) - 1 - axis_at))
    return loudness


def scatter_about(own_key, extent, spread, reach, shards=(), dtype=jnp.bfloat16):
    gain = shard_levels(own_key, extent, shards, -0.22, 0.18) if shards else 1.0
    entries = jax.random.normal(own_key, extent, jnp.float32) * spread * gain
    return jnp.minimum(jnp.maximum(entries, -reach), reach).astype(dtype)


def noise_with(stream_key, extent, scale, limit, split, heavy, dtype=jnp.bfloat16):
    values = scale * jax.random.normal(stream_key, extent, jnp.float32)
    if split:
        values = values * shard_levels(stream_key, extent, split, -0.22, 0.18)
    return jnp.clip(spiked(values, jax.random.fold_in(stream_key, 3), *heavy), -limit, limit).astype(dtype)


def setup_inputs(seed: int = 0) -> dict:
    key_of = jax.random.split(jax.random.key(seed), 8)
    anchor = scatter_about(key_of[0], (D, KV), 1.0, 6.0, ((0, 32),))
    pseudo_grads = scatter_about(key_of[1], (GROUPS, D, KV), 0.25, 1.5, ((0, 4), (1, 32)))
    outer_moment = scatter_about(key_of[2], (D, KV), 0.2, 1.2, ((0, 32),), jnp.float32)
    adam_first = scatter_about(key_of[3], (GROUPS, D, KV), 0.3, 1.8, ((0, 4), (1, 32)), jnp.float32)
    adam_second = jnp.clip(jnp.exp(math.log(4.0) - 2.7725887 * jax.random.uniform(key_of[4], (GROUPS, D, KV), jnp.float32) ** shard_levels(key_of[4], (GROUPS, D, KV), ((0, 4), (1, 32)), -0.2, 0.2)), 0.25, 4.0)
    inputs = noise_with(key_of[5], (TOKENS, D), 1.0, 24.0, ((0, 128),), (0, 1, 128, 5.5))
    key_cotangent = scatter_about(key_of[6], (TOKENS, KV), 1.0, 6.0, ((0, 128),))
    return dict(anchor=anchor, pseudo_grads=pseudo_grads, outer_moment=outer_moment, adam_first=adam_first, adam_second=adam_second, inputs=inputs, key_cotangent=key_cotangent)


OUTER_RATE = 0.7
MOMENTUM = 0.9
INNER_RATE = 0.05
BETA_ONE = 0.9
BETA_TWO = 0.95
ADAM_EPS = 1e-08
DECAY = 0.1
ADAM_STEP = 100

def reference(anchor, pseudo_grads, outer_moment, adam_first, adam_second, inputs, key_cotangent):
    scale = D ** (-0.5)
    mean_delta = lax.optimization_barrier(jnp.sum(pseudo_grads.astype(jnp.float32), axis=0)) / N_GROUP
    new_moment = MOMENTUM * outer_moment + mean_delta
    new_anchor = (anchor.astype(jnp.float32) - OUTER_RATE * (mean_delta + MOMENTUM * new_moment)).astype(jnp.bfloat16)
    cot_blocks = key_cotangent.reshape(N_GROUP * N_FSDP, TOK_DEV, KV)

    def input_block(block):
        return (jnp.dot(block, new_anchor.T, preferred_element_type=jnp.float32) * scale).astype(jnp.bfloat16)
    input_grad = lax.map(input_block, cot_blocks).reshape(N_GROUP * N_FSDP * TOK_DEV, D)
    in_blocks = inputs.reshape(N_GROUP, N_FSDP, TOK_DEV, D)
    cot_groups = key_cotangent.reshape(N_GROUP, N_FSDP, TOK_DEV, KV)

    def worker(pair):
        x_worker, k_worker = pair

        def add_block(total, block):
            x_block, k_block = block
            part = (jnp.dot(x_block.T, k_block, preferred_element_type=jnp.float32) * scale).astype(jnp.bfloat16)
            part = lax.optimization_barrier(part)
            return (total + part.astype(jnp.float32), None)
        total, unused = lax.scan(add_block, jnp.zeros((D, KV), jnp.float32), (x_worker, k_worker))
        return total
    grads = lax.map(worker, (in_blocks, cot_groups))
    correct_one = 1.0 - BETA_ONE ** ADAM_STEP
    correct_two = 1.0 - BETA_TWO ** ADAM_STEP
    first_moment = BETA_ONE * adam_first + (1.0 - BETA_ONE) * grads
    second_moment = BETA_TWO * adam_second + (1.0 - BETA_TWO) * grads * grads
    base = new_anchor.astype(jnp.float32)[None]
    step_size = first_moment / correct_one / (jnp.sqrt(second_moment / correct_two) + ADAM_EPS)
    inner_weights = (base * (1.0 - INNER_RATE * DECAY) - INNER_RATE * step_size).astype(jnp.bfloat16)
    return (new_anchor, new_moment, inner_weights, first_moment, second_moment, input_grad)
```

```python
import jax
import jax.numpy as jnp
from jax import lax
from jax.sharding import PartitionSpec as P

OUTER_RATE = 0.7
MOMENTUM = 0.9
INNER_RATE = 0.05
BETA_ONE = 0.9
BETA_TWO = 0.95
ADAM_EPS = 1e-08
DECAY = 0.1
ADAM_STEP = 100


def per_device(anchor, pseudo_grads, outer_moment, adam_first, adam_second, inputs, key_cotangent):
    width = inputs.shape[1]
    scale = width ** (-0.5)
    workers = lax.axis_size("group")

    cot_full = lax.all_gather(key_cotangent, "fsdp", axis=0, tiled=True)
    inputs_cols = lax.all_to_all(inputs, "fsdp", split_axis=1, concat_axis=0, tiled=True)

    total = lax.psum(pseudo_grads[0], "group").astype(jnp.float32)
    mean_delta = total / workers
    new_moment = MOMENTUM * outer_moment + mean_delta
    new_anchor = (
        anchor.astype(jnp.float32) - OUTER_RATE * (mean_delta + MOMENTUM * new_moment)
    ).astype(jnp.bfloat16)

    product = jnp.einsum("tk,dk->td", cot_full, new_anchor, preferred_element_type=jnp.float32)
    input_cols = (product * scale).astype(jnp.bfloat16)
    input_grad = lax.all_to_all(input_cols, "fsdp", split_axis=0, concat_axis=1, tiled=True)

    grads = (
        jnp.einsum("td,tk->dk", inputs_cols, cot_full, preferred_element_type=jnp.float32) * scale
    )
    correct_one = 1.0 - BETA_ONE**ADAM_STEP
    correct_two = 1.0 - BETA_TWO**ADAM_STEP
    first_moment = BETA_ONE * adam_first[0] + (1.0 - BETA_ONE) * grads
    second_moment = BETA_TWO * adam_second[0] + (1.0 - BETA_TWO) * grads * grads
    step_size = first_moment / correct_one / (jnp.sqrt(second_moment / correct_two) + ADAM_EPS)
    inner_weights = (
        new_anchor.astype(jnp.float32) * (1.0 - INNER_RATE * DECAY) - INNER_RATE * step_size
    ).astype(jnp.bfloat16)
    return (
        new_anchor,
        new_moment,
        inner_weights[None],
        first_moment[None],
        second_moment[None],
        input_grad,
    )


def solution(mesh):
    return jax.shard_map(
        per_device,
        mesh=mesh,
        in_specs=(
            P("fsdp", None),
            P("group", "fsdp", None),
            P("fsdp", None),
            P("group", "fsdp", None),
            P("group", "fsdp", None),
            P(("group", "fsdp"), None),
            P(("group", "fsdp"), None),
        ),
        out_specs=(
            P("fsdp", None),
            P("fsdp", None),
            P("group", "fsdp", None),
            P("group", "fsdp", None),
            P("group", "fsdp", None),
            P(("group", "fsdp"), None),
        ),
        check_vma=False,
    )
```

```python
import jax
import jax.numpy as jnp
from jax import lax
from jax.sharding import Mesh
from jax.sharding import PartitionSpec as P

OUTER_RATE = 0.7
MOMENTUM = 0.9
INNER_RATE = 0.05
BETA_ONE = 0.9
BETA_TWO = 0.95
ADAM_EPS = 1e-08
DECAY = 0.1
ADAM_STEP = 100

GROUP = ("y_lo", "core")
TEAMS = ("y_hi", "x")
TEAM = "z"
FSDP = TEAMS + (TEAM,)


def per_device(anchor, pseudo_grads, outer_moment, adam_first, adam_second, inputs, key_cotangent):
    tok, width = inputs.shape
    rows, kv = anchor.shape
    scale = width ** (-0.5)
    workers = lax.axis_size(GROUP)
    teams = lax.axis_size(TEAMS)
    team = lax.axis_size(TEAM)

    cot_team = lax.all_gather(key_cotangent, TEAM, axis=0, tiled=True)
    inputs_part = lax.all_to_all(
        inputs.reshape(tok, teams, team, rows), TEAM, split_axis=2, concat_axis=0, tiled=True
    ).reshape(team * tok, teams * rows)

    total = lax.psum(pseudo_grads[0], GROUP).astype(jnp.float32)
    mean_delta = total / workers
    new_moment = MOMENTUM * outer_moment + mean_delta
    new_anchor = (
        anchor.astype(jnp.float32) - OUTER_RATE * (mean_delta + MOMENTUM * new_moment)
    ).astype(jnp.bfloat16)
    new_anchor = lax.optimization_barrier(new_anchor)

    anchor_part = lax.all_gather(new_anchor, TEAMS, axis=0, tiled=True)
    product = jnp.einsum("tk,dk->td", cot_team, anchor_part, preferred_element_type=jnp.float32)
    input_part = (product * scale).astype(jnp.bfloat16)
    input_grad = lax.all_to_all(
        input_part.reshape(team, tok, teams, 1, rows), TEAM, split_axis=0, concat_axis=3, tiled=True
    ).reshape(tok, width)

    partial = (
        jnp.einsum("td,tk->dk", inputs_part, cot_team, preferred_element_type=jnp.float32) * scale
    ).astype(jnp.bfloat16)
    grads = lax.psum_scatter(partial, TEAMS, scatter_dimension=0, tiled=True).astype(jnp.float32)

    correct_one = 1.0 - BETA_ONE**ADAM_STEP
    correct_two = 1.0 - BETA_TWO**ADAM_STEP
    first_moment = BETA_ONE * adam_first[0] + (1.0 - BETA_ONE) * grads
    second_moment = BETA_TWO * adam_second[0] + (1.0 - BETA_TWO) * grads * grads
    step_size = first_moment / correct_one / (jnp.sqrt(second_moment / correct_two) + ADAM_EPS)
    inner_weights = (
        new_anchor.astype(jnp.float32) * (1.0 - INNER_RATE * DECAY) - INNER_RATE * step_size
    ).astype(jnp.bfloat16)
    return (
        new_anchor,
        new_moment,
        inner_weights[None],
        first_moment[None],
        second_moment[None],
        input_grad,
    )


def physical_mesh(mesh):
    groups = mesh.shape["group"]
    shards = mesh.shape["fsdp"]
    cores = 2
    y_hi = 2
    x = int(round((shards // y_hi) ** 0.5))
    devices = mesh.devices.reshape(groups // cores, cores, y_hi, x, shards // (y_hi * x))
    return Mesh(devices, GROUP + FSDP)


def solution(mesh):
    pmesh = physical_mesh(mesh)
    rows = P(FSDP, None)
    stacked = P(GROUP, FSDP, None)
    tokens = P(GROUP + FSDP, None)
    return jax.shard_map(
        per_device,
        mesh=pmesh,
        in_specs=(rows, stacked, rows, stacked, stacked, tokens, tokens),
        out_specs=(rows, rows, stacked, stacked, stacked, tokens),
        check_vma=False,
    )
```

```python
import jax
import jax.numpy as jnp
from jax import lax
from jax.sharding import Mesh
from jax.sharding import PartitionSpec as P

OUTER_RATE = 0.7
MOMENTUM = 0.9
INNER_RATE = 0.05
BETA_ONE = 0.9
BETA_TWO = 0.95
ADAM_EPS = 1e-08
DECAY = 0.1
ADAM_STEP = 100

GROUP = ("y_lo", "core")
TEAMS = ("y_hi", "x")
TEAM = "z"
FSDP = TEAMS + (TEAM,)


def per_device(anchor, pseudo_grads, outer_moment, adam_first, adam_second, inputs, key_cotangent):
    tok, width = inputs.shape
    rows, kv = anchor.shape
    scale = width ** (-0.5)
    workers = lax.axis_size(GROUP)
    teams = lax.axis_size(TEAMS)
    team = lax.axis_size(TEAM)

    cot_team = lax.all_gather(key_cotangent, TEAM, axis=0, tiled=True)
    inputs_part = lax.all_to_all(
        inputs.reshape(tok, teams, team, rows), TEAM, split_axis=2, concat_axis=0, tiled=True
    ).reshape(team * tok, teams * rows)

    own = pseudo_grads[0]
    pair = own.astype(jnp.float32) + lax.ppermute(own, "y_lo", perm=[(0, 1), (1, 0)]).astype(
        jnp.float32
    )
    total = pair + lax.ppermute(pair, "core", perm=[(0, 1), (1, 0)])
    mean_delta = total / workers
    new_moment = MOMENTUM * outer_moment + mean_delta
    new_anchor = (
        anchor.astype(jnp.float32) - OUTER_RATE * (mean_delta + MOMENTUM * new_moment)
    ).astype(jnp.bfloat16)
    new_anchor = lax.optimization_barrier(new_anchor)

    half = kv // 2
    core = lax.axis_index("core")
    mine = lax.all_gather(
        lax.dynamic_slice_in_dim(new_anchor, core * half, half, axis=1), TEAMS, axis=0, tiled=True
    )
    other = lax.ppermute(mine, "core", perm=[(0, 1), (1, 0)])
    cot_mine = lax.dynamic_slice_in_dim(cot_team, core * half, half, axis=1)
    cot_other = lax.dynamic_slice_in_dim(cot_team, (1 - core) * half, half, axis=1)
    product = jnp.einsum(
        "tk,dk->td", cot_mine, mine, preferred_element_type=jnp.float32
    ) + jnp.einsum("tk,dk->td", cot_other, other, preferred_element_type=jnp.float32)
    input_part = (product * scale).astype(jnp.bfloat16)
    input_grad = lax.all_to_all(
        input_part.reshape(team, tok, teams, 1, rows), TEAM, split_axis=0, concat_axis=3, tiled=True
    ).reshape(tok, width)

    partial = (
        jnp.einsum("td,tk->dk", inputs_part, cot_team, preferred_element_type=jnp.float32) * scale
    ).astype(jnp.bfloat16)
    grads = lax.psum_scatter(partial, TEAMS, scatter_dimension=0, tiled=True).astype(jnp.float32)

    correct_one = 1.0 - BETA_ONE**ADAM_STEP
    correct_two = 1.0 - BETA_TWO**ADAM_STEP
    first_moment = BETA_ONE * adam_first[0] + (1.0 - BETA_ONE) * grads
    second_moment = BETA_TWO * adam_second[0] + (1.0 - BETA_TWO) * grads * grads
    step_size = first_moment / correct_one / (jnp.sqrt(second_moment / correct_two) + ADAM_EPS)
    inner_weights = (
        new_anchor.astype(jnp.float32) * (1.0 - INNER_RATE * DECAY) - INNER_RATE * step_size
    ).astype(jnp.bfloat16)
    return (
        new_anchor,
        new_moment,
        inner_weights[None],
        first_moment[None],
        second_moment[None],
        input_grad,
    )


def physical_mesh(mesh):
    groups = mesh.shape["group"]
    shards = mesh.shape["fsdp"]
    cores = 2
    y_hi = 2
    x = int(round((shards // y_hi) ** 0.5))
    devices = mesh.devices.reshape(groups // cores, cores, y_hi, x, shards // (y_hi * x))
    return Mesh(devices, GROUP + FSDP)


def solution(mesh):
    pmesh = physical_mesh(mesh)
    rows = P(FSDP, None)
    stacked = P(GROUP, FSDP, None)
    tokens = P(GROUP + FSDP, None)
    return jax.shard_map(
        per_device,
        mesh=pmesh,
        in_specs=(rows, stacked, rows, stacked, stacked, tokens, tokens),
        out_specs=(rows, rows, stacked, stacked, stacked, tokens),
        check_vma=False,
    )
```

```python
import jax
import jax.numpy as jnp
from jax import lax
from jax.sharding import Mesh
from jax.sharding import PartitionSpec as P

OUTER_RATE = 0.7
MOMENTUM = 0.9
INNER_RATE = 0.05
BETA_ONE = 0.9
BETA_TWO = 0.95
ADAM_EPS = 1e-08
DECAY = 0.1
ADAM_STEP = 100

GROUP = ("y_lo", "core")
TEAMS = ("y_hi", "x")
TEAM = "z"
FSDP = TEAMS + (TEAM,)


def per_device(anchor, pseudo_grads, outer_moment, adam_first, adam_second, inputs, key_cotangent):
    tok, width = inputs.shape
    rows, kv = anchor.shape
    scale = width ** (-0.5)
    workers = lax.axis_size(GROUP)
    teams = lax.axis_size(TEAMS)
    team = lax.axis_size(TEAM)

    chunks = kv // rows
    cols = inputs.reshape(tok, teams, team, rows).transpose(2, 1, 0, 3)
    cot_chunks = key_cotangent.reshape(tok, chunks, rows).transpose(1, 0, 2)
    cot_chunks = jnp.broadcast_to(cot_chunks[None], (team,) + cot_chunks.shape)
    sent = jnp.concatenate([cols, cot_chunks], axis=1)
    got = lax.all_to_all(sent, TEAM, split_axis=0, concat_axis=0, tiled=True)
    inputs_part = got[:, :teams]
    cot_team = got[:, teams:].transpose(0, 2, 1, 3).reshape(team * tok, kv)

    own = pseudo_grads[0]
    pair = own.astype(jnp.float32) + lax.ppermute(own, "y_lo", perm=[(0, 1), (1, 0)]).astype(
        jnp.float32
    )
    total = pair + lax.ppermute(pair, "core", perm=[(0, 1), (1, 0)])
    mean_delta = total / workers
    new_moment = MOMENTUM * outer_moment + mean_delta
    new_anchor = (
        anchor.astype(jnp.float32) - OUTER_RATE * (mean_delta + MOMENTUM * new_moment)
    ).astype(jnp.bfloat16)
    new_anchor = lax.optimization_barrier(new_anchor)

    half = kv // 2
    core = lax.axis_index("core")
    mine = lax.all_gather(
        lax.dynamic_slice_in_dim(new_anchor, core * half, half, axis=1), TEAMS, axis=0, tiled=True
    )
    other = lax.ppermute(mine, "core", perm=[(0, 1), (1, 0)])
    cot_mine = lax.dynamic_slice_in_dim(cot_team, core * half, half, axis=1)
    cot_other = lax.dynamic_slice_in_dim(cot_team, (1 - core) * half, half, axis=1)
    product = jnp.einsum(
        "tk,dk->td", cot_mine, mine, preferred_element_type=jnp.float32
    ) + jnp.einsum("tk,dk->td", cot_other, other, preferred_element_type=jnp.float32)
    input_part = (product * scale).astype(jnp.bfloat16).reshape(team, tok, teams * rows)
    input_grad = (
        lax.all_to_all(input_part, TEAM, split_axis=0, concat_axis=0, tiled=True)
        .reshape(team, tok, teams, rows)
        .transpose(1, 2, 0, 3)
        .reshape(tok, width)
    )

    partial = (
        jnp.einsum(
            "satr,stk->ark",
            inputs_part,
            cot_team.reshape(team, tok, kv),
            preferred_element_type=jnp.float32,
        )
        * scale
    ).astype(jnp.bfloat16).reshape(teams * rows, kv)
    grads = lax.psum_scatter(partial, TEAMS, scatter_dimension=0, tiled=True).astype(jnp.float32)

    correct_one = 1.0 - BETA_ONE**ADAM_STEP
    correct_two = 1.0 - BETA_TWO**ADAM_STEP
    first_moment = BETA_ONE * adam_first[0] + (1.0 - BETA_ONE) * grads
    second_moment = BETA_TWO * adam_second[0] + (1.0 - BETA_TWO) * grads * grads
    step_size = first_moment / correct_one / (jnp.sqrt(second_moment / correct_two) + ADAM_EPS)
    inner_weights = (
        new_anchor.astype(jnp.float32) * (1.0 - INNER_RATE * DECAY) - INNER_RATE * step_size
    ).astype(jnp.bfloat16)
    return (
        new_anchor,
        new_moment,
        inner_weights[None],
        first_moment[None],
        second_moment[None],
        input_grad,
    )


def physical_mesh(mesh):
    groups = mesh.shape["group"]
    shards = mesh.shape["fsdp"]
    cores = 2
    y_hi = 2
    x = int(round((shards // y_hi) ** 0.5))
    devices = mesh.devices.reshape(groups // cores, cores, y_hi, x, shards // (y_hi * x))
    return Mesh(devices, GROUP + FSDP)


def solution(mesh):
    pmesh = physical_mesh(mesh)
    rows = P(FSDP, None)
    stacked = P(GROUP, FSDP, None)
    tokens = P(GROUP + FSDP, None)
    return jax.shard_map(
        per_device,
        mesh=pmesh,
        in_specs=(rows, stacked, rows, stacked, stacked, tokens, tokens),
        out_specs=(rows, rows, stacked, stacked, stacked, tokens),
        check_vma=False,
    )
```

```python
import jax
import jax.numpy as jnp
from jax import lax
from jax.sharding import Mesh
from jax.sharding import PartitionSpec as P

OUTER_RATE = 0.7
MOMENTUM = 0.9
INNER_RATE = 0.05
BETA_ONE = 0.9
BETA_TWO = 0.95
ADAM_EPS = 1e-08
DECAY = 0.1
ADAM_STEP = 100

GROUP = ("y_lo", "core")
TEAMS = ("y_hi", "x")
TEAM = "z"
FSDP = TEAMS + (TEAM,)


def per_device(anchor, pseudo_grads, outer_moment, adam_first, adam_second, inputs, key_cotangent):
    tok, width = inputs.shape
    rows, kv = anchor.shape
    scale = width ** (-0.5)
    workers = lax.axis_size(GROUP)
    teams = lax.axis_size(TEAMS)
    team = lax.axis_size(TEAM)

    chunks = kv // rows
    cols = inputs.reshape(tok, teams, team, rows).transpose(2, 1, 0, 3)
    cot_chunks = key_cotangent.reshape(tok, chunks, rows).transpose(1, 0, 2)
    cot_chunks = jnp.broadcast_to(cot_chunks[None], (team,) + cot_chunks.shape)
    sent = jnp.concatenate([cols, cot_chunks], axis=1)
    own = pseudo_grads[0]
    pair = own.astype(jnp.float32) + lax.ppermute(own, "y_lo", perm=[(0, 1), (1, 0)]).astype(
        jnp.float32
    )
    total = pair + lax.ppermute(pair, "core", perm=[(0, 1), (1, 0)])
    mean_delta = total / workers
    new_moment = MOMENTUM * outer_moment + mean_delta
    new_anchor = (
        anchor.astype(jnp.float32) - OUTER_RATE * (mean_delta + MOMENTUM * new_moment)
    ).astype(jnp.bfloat16)
    sent, new_anchor = lax.optimization_barrier((sent, new_anchor))
    got = lax.all_to_all(sent, TEAM, split_axis=0, concat_axis=0, tiled=True)
    inputs_part = got[:, :teams]
    cot_team = got[:, teams:].transpose(0, 2, 1, 3).reshape(team * tok, kv)

    half = kv // 2
    core = lax.axis_index("core")
    mine = lax.all_gather(
        lax.dynamic_slice_in_dim(new_anchor, core * half, half, axis=1), TEAMS, axis=0, tiled=True
    )
    other = lax.ppermute(mine, "core", perm=[(0, 1), (1, 0)])
    cot_mine = lax.dynamic_slice_in_dim(cot_team, core * half, half, axis=1)
    cot_other = lax.dynamic_slice_in_dim(cot_team, (1 - core) * half, half, axis=1)
    product = jnp.einsum(
        "tk,dk->td", cot_mine, mine, preferred_element_type=jnp.float32
    ) + jnp.einsum("tk,dk->td", cot_other, other, preferred_element_type=jnp.float32)
    input_part = (product * scale).astype(jnp.bfloat16).reshape(team, tok, teams * rows)
    input_grad = (
        lax.all_to_all(input_part, TEAM, split_axis=0, concat_axis=0, tiled=True)
        .reshape(team, tok, teams, rows)
        .transpose(1, 2, 0, 3)
        .reshape(tok, width)
    )

    partial = (
        jnp.einsum(
            "satr,stk->ark",
            inputs_part,
            cot_team.reshape(team, tok, kv),
            preferred_element_type=jnp.float32,
        )
        * scale
    ).astype(jnp.bfloat16).reshape(teams * rows, kv)
    grads = lax.psum_scatter(partial, TEAMS, scatter_dimension=0, tiled=True).astype(jnp.float32)

    correct_one = 1.0 - BETA_ONE**ADAM_STEP
    correct_two = 1.0 - BETA_TWO**ADAM_STEP
    first_moment = BETA_ONE * adam_first[0] + (1.0 - BETA_ONE) * grads
    second_moment = BETA_TWO * adam_second[0] + (1.0 - BETA_TWO) * grads * grads
    step_size = first_moment / correct_one / (jnp.sqrt(second_moment / correct_two) + ADAM_EPS)
    inner_weights = (
        new_anchor.astype(jnp.float32) * (1.0 - INNER_RATE * DECAY) - INNER_RATE * step_size
    ).astype(jnp.bfloat16)
    return (
        new_anchor,
        new_moment,
        inner_weights[None],
        first_moment[None],
        second_moment[None],
        input_grad,
    )


def physical_mesh(mesh):
    groups = mesh.shape["group"]
    shards = mesh.shape["fsdp"]
    cores = 2
    y_hi = 2
    x = int(round((shards // y_hi) ** 0.5))
    devices = mesh.devices.reshape(groups // cores, cores, y_hi, x, shards // (y_hi * x))
    return Mesh(devices, GROUP + FSDP)


def solution(mesh):
    pmesh = physical_mesh(mesh)
    rows = P(FSDP, None)
    stacked = P(GROUP, FSDP, None)
    tokens = P(GROUP + FSDP, None)
    return jax.shard_map(
        per_device,
        mesh=pmesh,
        in_specs=(rows, stacked, rows, stacked, stacked, tokens, tokens),
        out_specs=(rows, rows, stacked, stacked, stacked, tokens),
        check_vma=False,
    )
```

```python
import jax
import jax.numpy as jnp
from jax import lax
from jax.sharding import Mesh
from jax.sharding import PartitionSpec as P

OUTER_RATE = 0.7
MOMENTUM = 0.9
INNER_RATE = 0.05
BETA_ONE = 0.9
BETA_TWO = 0.95
ADAM_EPS = 1e-08
DECAY = 0.1
ADAM_STEP = 100

GROUP = ("y_lo", "core")
TEAMS = ("y_hi", "x")
TEAM = "z"
FSDP = TEAMS + (TEAM,)


def per_device(anchor, pseudo_grads, outer_moment, adam_first, adam_second, inputs, key_cotangent):
    tok, width = inputs.shape
    rows, kv = anchor.shape
    scale = width ** (-0.5)
    workers = lax.axis_size(GROUP)
    teams = lax.axis_size(TEAMS)
    team = lax.axis_size(TEAM)

    chunks = kv // rows
    cols = inputs.reshape(tok, teams, team, rows).transpose(2, 1, 0, 3)
    cot_chunks = key_cotangent.reshape(tok, chunks, rows).transpose(1, 0, 2)
    cot_chunks = jnp.broadcast_to(cot_chunks[None], (team,) + cot_chunks.shape)
    sent = jnp.concatenate([cols, cot_chunks], axis=1)
    got = lax.all_to_all(sent, TEAM, split_axis=0, concat_axis=0, tiled=True)
    inputs_part = got[:, :teams]
    cot_team = got[:, teams:].transpose(0, 2, 1, 3).reshape(team * tok, kv)

    own = pseudo_grads[0]
    pair = own.astype(jnp.float32) + lax.ppermute(own, "y_lo", perm=[(0, 1), (1, 0)]).astype(
        jnp.float32
    )
    total = pair + lax.ppermute(pair, "core", perm=[(0, 1), (1, 0)])
    mean_delta = total / workers
    new_moment = MOMENTUM * outer_moment + mean_delta
    new_anchor = (
        anchor.astype(jnp.float32) - OUTER_RATE * (mean_delta + MOMENTUM * new_moment)
    ).astype(jnp.bfloat16)
    new_anchor = lax.optimization_barrier(new_anchor)

    half = kv // 2
    core = lax.axis_index("core")
    mine = lax.all_gather(
        lax.dynamic_slice_in_dim(new_anchor, core * half, half, axis=1), TEAMS, axis=0, tiled=True
    )
    other = lax.ppermute(mine, "core", perm=[(0, 1), (1, 0)])
    cot_mine = lax.dynamic_slice_in_dim(cot_team, core * half, half, axis=1)
    cot_other = lax.dynamic_slice_in_dim(cot_team, (1 - core) * half, half, axis=1)
    product = jnp.einsum(
        "tk,dk->td", cot_mine, mine, preferred_element_type=jnp.float32
    ) + jnp.einsum("tk,dk->td", cot_other, other, preferred_element_type=jnp.float32)
    input_part = (product * scale).astype(jnp.bfloat16).reshape(team, tok, teams * rows)
    input_grad = (
        lax.all_to_all(input_part, TEAM, split_axis=0, concat_axis=0, tiled=True)
        .reshape(team, tok, teams, rows)
        .transpose(1, 2, 0, 3)
        .reshape(tok, width)
    )

    partial = (
        jnp.einsum(
            "satr,stk->ark",
            inputs_part,
            cot_team.reshape(team, tok, kv),
            preferred_element_type=jnp.float32,
        )
        * scale
    ).astype(jnp.bfloat16)
    grads = jnp.sum(
        lax.all_to_all(partial, TEAMS, split_axis=0, concat_axis=0, tiled=True).astype(
            jnp.float32
        ),
        axis=0,
    )

    correct_one = 1.0 - BETA_ONE**ADAM_STEP
    correct_two = 1.0 - BETA_TWO**ADAM_STEP
    first_moment = BETA_ONE * adam_first[0] + (1.0 - BETA_ONE) * grads
    second_moment = BETA_TWO * adam_second[0] + (1.0 - BETA_TWO) * grads * grads
    step_size = first_moment / correct_one / (jnp.sqrt(second_moment / correct_two) + ADAM_EPS)
    inner_weights = (
        new_anchor.astype(jnp.float32) * (1.0 - INNER_RATE * DECAY) - INNER_RATE * step_size
    ).astype(jnp.bfloat16)
    return (
        new_anchor,
        new_moment,
        inner_weights[None],
        first_moment[None],
        second_moment[None],
        input_grad,
    )


def physical_mesh(mesh):
    groups = mesh.shape["group"]
    shards = mesh.shape["fsdp"]
    cores = 2
    y_hi = 2
    x = int(round((shards // y_hi) ** 0.5))
    devices = mesh.devices.reshape(groups // cores, cores, y_hi, x, shards // (y_hi * x))
    return Mesh(devices, GROUP + FSDP)


def solution(mesh):
    pmesh = physical_mesh(mesh)
    rows = P(FSDP, None)
    stacked = P(GROUP, FSDP, None)
    tokens = P(GROUP + FSDP, None)
    return jax.shard_map(
        per_device,
        mesh=pmesh,
        in_specs=(rows, stacked, rows, stacked, stacked, tokens, tokens),
        out_specs=(rows, rows, stacked, stacked, stacked, tokens),
        check_vma=False,
    )
```

```python
import jax
import jax.numpy as jnp
from jax import lax
from jax.sharding import Mesh
from jax.sharding import PartitionSpec as P

OUTER_RATE = 0.7
MOMENTUM = 0.9
INNER_RATE = 0.05
BETA_ONE = 0.9
BETA_TWO = 0.95
ADAM_EPS = 1e-08
DECAY = 0.1
ADAM_STEP = 100

GROUP = ("y_lo", "core")
TEAMS = ("y_hi", "x")
TEAM = "z"
FSDP = TEAMS + (TEAM,)


def per_device(anchor, pseudo_grads, outer_moment, adam_first, adam_second, inputs, key_cotangent):
    tok, width = inputs.shape
    rows, kv = anchor.shape
    scale = width ** (-0.5)
    workers = lax.axis_size(GROUP)
    teams = lax.axis_size(TEAMS)
    team = lax.axis_size(TEAM)

    cot_team = lax.all_gather(key_cotangent, TEAM, axis=0, tiled=True)
    inputs_part = lax.all_to_all(
        inputs.reshape(tok, teams, team, rows), TEAM, split_axis=2, concat_axis=0, tiled=True
    ).reshape(team * tok, teams * rows)

    own = pseudo_grads[0]
    pair = own.astype(jnp.float32) + lax.ppermute(own, "y_lo", perm=[(0, 1), (1, 0)]).astype(
        jnp.float32
    )
    total = pair + lax.ppermute(pair, "core", perm=[(0, 1), (1, 0)])
    mean_delta = total / workers
    new_moment = MOMENTUM * outer_moment + mean_delta
    new_anchor = (
        anchor.astype(jnp.float32) - OUTER_RATE * (mean_delta + MOMENTUM * new_moment)
    ).astype(jnp.bfloat16)
    new_anchor, cot_team = lax.optimization_barrier((new_anchor, cot_team))

    half = kv // 2
    core = lax.axis_index("core")
    mine = lax.all_gather(
        lax.dynamic_slice_in_dim(new_anchor, core * half, half, axis=1), FSDP, axis=0, tiled=True
    )
    other = lax.ppermute(mine, "core", perm=[(0, 1), (1, 0)])
    cot_mine = lax.dynamic_slice_in_dim(key_cotangent, core * half, half, axis=1)
    cot_other = lax.dynamic_slice_in_dim(key_cotangent, (1 - core) * half, half, axis=1)
    product = jnp.einsum(
        "tk,dk->td", cot_mine, mine, preferred_element_type=jnp.float32
    ) + jnp.einsum("tk,dk->td", cot_other, other, preferred_element_type=jnp.float32)
    input_grad = (product * scale).astype(jnp.bfloat16)

    partial = (
        jnp.einsum("td,tk->dk", inputs_part, cot_team, preferred_element_type=jnp.float32) * scale
    ).astype(jnp.bfloat16)
    grads = jnp.sum(
        lax.all_to_all(
            partial.reshape(teams, rows, kv), TEAMS, split_axis=0, concat_axis=0, tiled=True
        ).astype(jnp.float32),
        axis=0,
    )

    correct_one = 1.0 - BETA_ONE**ADAM_STEP
    correct_two = 1.0 - BETA_TWO**ADAM_STEP
    first_moment = BETA_ONE * adam_first[0] + (1.0 - BETA_ONE) * grads
    second_moment = BETA_TWO * adam_second[0] + (1.0 - BETA_TWO) * grads * grads
    step_size = first_moment / correct_one / (jnp.sqrt(second_moment / correct_two) + ADAM_EPS)
    inner_weights = (
        new_anchor.astype(jnp.float32) * (1.0 - INNER_RATE * DECAY) - INNER_RATE * step_size
    ).astype(jnp.bfloat16)
    return (
        new_anchor,
        new_moment,
        inner_weights[None],
        first_moment[None],
        second_moment[None],
        input_grad,
    )


def physical_mesh(mesh):
    groups = mesh.shape["group"]
    shards = mesh.shape["fsdp"]
    cores = 2
    y_hi = 2
    x = int(round((shards // y_hi) ** 0.5))
    devices = mesh.devices.reshape(groups // cores, cores, y_hi, x, shards // (y_hi * x))
    return Mesh(devices, GROUP + FSDP)


def solution(mesh):
    pmesh = physical_mesh(mesh)
    rows = P(FSDP, None)
    stacked = P(GROUP, FSDP, None)
    tokens = P(GROUP + FSDP, None)
    return jax.shard_map(
        per_device,
        mesh=pmesh,
        in_specs=(rows, stacked, rows, stacked, stacked, tokens, tokens),
        out_specs=(rows, rows, stacked, stacked, stacked, tokens),
        check_vma=False,
    )
```

```python
import jax
import jax.numpy as jnp
from jax import lax
from jax.sharding import Mesh
from jax.sharding import PartitionSpec as P

OUTER_RATE = 0.7
MOMENTUM = 0.9
INNER_RATE = 0.05
BETA_ONE = 0.9
BETA_TWO = 0.95
ADAM_EPS = 1e-08
DECAY = 0.1
ADAM_STEP = 100

GROUP = ("y_lo", "core")
FSDP = ("y_hi", "x", "z")
TEAMS = "x"
TEAM = ("y_hi", "z")


def per_device(anchor, pseudo_grads, outer_moment, adam_first, adam_second, inputs, key_cotangent):
    tok, width = inputs.shape
    rows, kv = anchor.shape
    scale = width ** (-0.5)
    workers = lax.axis_size(GROUP)
    teams = lax.axis_size(TEAMS)
    team = lax.axis_size(TEAM)

    cot_team = lax.all_gather(key_cotangent, TEAM, axis=0, tiled=True)
    hi = lax.axis_size("y_hi")
    lo = lax.axis_size("z")
    cols = inputs.reshape(tok, hi, teams, lo, rows).transpose(0, 2, 1, 3, 4)
    inputs_part = lax.all_to_all(
        cols.reshape(tok, teams, team, rows), TEAM, split_axis=2, concat_axis=0, tiled=True
    ).reshape(team * tok, teams * rows)

    own = pseudo_grads[0]
    pair = own.astype(jnp.float32) + lax.ppermute(own, "y_lo", perm=[(0, 1), (1, 0)]).astype(
        jnp.float32
    )
    total = pair + lax.ppermute(pair, "core", perm=[(0, 1), (1, 0)])
    mean_delta = total / workers
    new_moment = MOMENTUM * outer_moment + mean_delta
    new_anchor = (
        anchor.astype(jnp.float32) - OUTER_RATE * (mean_delta + MOMENTUM * new_moment)
    ).astype(jnp.bfloat16)
    new_anchor = lax.optimization_barrier(new_anchor)

    half = kv // 2
    core = lax.axis_index("core")
    mine = lax.all_gather(
        lax.dynamic_slice_in_dim(new_anchor, core * half, half, axis=1), TEAMS, axis=0, tiled=True
    )
    other = lax.ppermute(mine, "core", perm=[(0, 1), (1, 0)])
    cot_mine = lax.dynamic_slice_in_dim(cot_team, core * half, half, axis=1)
    cot_other = lax.dynamic_slice_in_dim(cot_team, (1 - core) * half, half, axis=1)
    product = jnp.einsum(
        "tk,dk->td", cot_mine, mine, preferred_element_type=jnp.float32
    ) + jnp.einsum("tk,dk->td", cot_other, other, preferred_element_type=jnp.float32)
    input_part = (product * scale).astype(jnp.bfloat16).reshape(team, tok, teams, rows)
    input_grad = (
        lax.all_to_all(input_part, TEAM, split_axis=0, concat_axis=0, tiled=True)
        .reshape(hi, lo, tok, teams, rows)
        .transpose(2, 0, 3, 1, 4)
        .reshape(tok, width)
    )

    partial = (
        jnp.einsum("td,tk->dk", inputs_part, cot_team, preferred_element_type=jnp.float32) * scale
    ).astype(jnp.bfloat16)
    grads = lax.psum_scatter(partial, TEAMS, scatter_dimension=0, tiled=True).astype(jnp.float32)

    correct_one = 1.0 - BETA_ONE**ADAM_STEP
    correct_two = 1.0 - BETA_TWO**ADAM_STEP
    first_moment = BETA_ONE * adam_first[0] + (1.0 - BETA_ONE) * grads
    second_moment = BETA_TWO * adam_second[0] + (1.0 - BETA_TWO) * grads * grads
    step_size = first_moment / correct_one / (jnp.sqrt(second_moment / correct_two) + ADAM_EPS)
    inner_weights = (
        new_anchor.astype(jnp.float32) * (1.0 - INNER_RATE * DECAY) - INNER_RATE * step_size
    ).astype(jnp.bfloat16)
    return (
        new_anchor,
        new_moment,
        inner_weights[None],
        first_moment[None],
        second_moment[None],
        input_grad,
    )


def physical_mesh(mesh):
    groups = mesh.shape["group"]
    shards = mesh.shape["fsdp"]
    cores = 2
    y_hi = 2
    x = int(round((shards // y_hi) ** 0.5))
    devices = mesh.devices.reshape(groups // cores, cores, y_hi, x, shards // (y_hi * x))
    return Mesh(devices, GROUP + FSDP)


def solution(mesh):
    pmesh = physical_mesh(mesh)
    rows = P(FSDP, None)
    stacked = P(GROUP, FSDP, None)
    tokens = P(GROUP + FSDP, None)
    return jax.shard_map(
        per_device,
        mesh=pmesh,
        in_specs=(rows, stacked, rows, stacked, stacked, tokens, tokens),
        out_specs=(rows, rows, stacked, stacked, stacked, tokens),
        check_vma=False,
    )
```

```python
import jax
import jax.numpy as jnp
from jax import lax
from jax.sharding import Mesh
from jax.sharding import PartitionSpec as P

OUTER_RATE = 0.7
MOMENTUM = 0.9
INNER_RATE = 0.05
BETA_ONE = 0.9
BETA_TWO = 0.95
ADAM_EPS = 1e-08
DECAY = 0.1
ADAM_STEP = 100

GROUP = ("y_lo", "core")
TEAMS = ("y_hi", "x")
TEAM = "z"
FSDP = TEAMS + (TEAM,)


def per_device(anchor, pseudo_grads, outer_moment, adam_first, adam_second, inputs, key_cotangent):
    tok, width = inputs.shape
    rows, kv = anchor.shape
    scale = width ** (-0.5)
    workers = lax.axis_size(GROUP)
    teams = lax.axis_size(TEAMS)
    team = lax.axis_size(TEAM)

    cot_team = lax.all_gather(key_cotangent, TEAM, axis=0, tiled=True)
    inputs_part = lax.all_to_all(
        inputs.reshape(tok, teams, team, rows), TEAM, split_axis=2, concat_axis=0, tiled=True
    ).reshape(team * tok, teams * rows)

    own = pseudo_grads[0]
    pair = own.astype(jnp.float32) + lax.ppermute(own, "y_lo", perm=[(0, 1), (1, 0)]).astype(
        jnp.float32
    )
    total = pair + lax.ppermute(pair, "core", perm=[(0, 1), (1, 0)])
    mean_delta = total / workers
    new_moment = MOMENTUM * outer_moment + mean_delta
    new_anchor = (
        anchor.astype(jnp.float32) - OUTER_RATE * (mean_delta + MOMENTUM * new_moment)
    ).astype(jnp.bfloat16)
    new_anchor = lax.optimization_barrier(new_anchor)

    half = kv // 2
    core = lax.axis_index("core")
    mine = lax.all_gather(
        lax.dynamic_slice_in_dim(new_anchor, core * half, half, axis=1), TEAMS, axis=0, tiled=True
    )
    other = lax.ppermute(mine, "core", perm=[(0, 1), (1, 0)])
    cot_mine = lax.dynamic_slice_in_dim(cot_team, core * half, half, axis=1)
    cot_other = lax.dynamic_slice_in_dim(cot_team, (1 - core) * half, half, axis=1)
    product = jnp.einsum(
        "tk,dk->td", cot_mine, mine, preferred_element_type=jnp.float32
    ) + jnp.einsum("tk,dk->td", cot_other, other, preferred_element_type=jnp.float32)
    input_part = (product * scale).astype(jnp.bfloat16)
    input_grad = lax.all_to_all(
        input_part.reshape(team, tok, teams, 1, rows), TEAM, split_axis=0, concat_axis=3, tiled=True
    ).reshape(tok, width)

    partial = (
        jnp.einsum("td,tk->dk", inputs_part, cot_team, preferred_element_type=jnp.float32) * scale
    ).astype(jnp.bfloat16)
    halves = partial.reshape(lax.axis_size("y_hi"), -1, kv)
    y = lax.axis_index("y_hi")
    kept = lax.dynamic_index_in_dim(halves, y, axis=0, keepdims=False)
    given = lax.dynamic_index_in_dim(halves, 1 - y, axis=0, keepdims=False)
    paired = (
        kept.astype(jnp.float32)
        + lax.ppermute(given, "y_hi", perm=[(0, 1), (1, 0)]).astype(jnp.float32)
    ).astype(jnp.bfloat16)
    grads = lax.psum_scatter(paired, "x", scatter_dimension=0, tiled=True).astype(jnp.float32)

    correct_one = 1.0 - BETA_ONE**ADAM_STEP
    correct_two = 1.0 - BETA_TWO**ADAM_STEP
    first_moment = BETA_ONE * adam_first[0] + (1.0 - BETA_ONE) * grads
    second_moment = BETA_TWO * adam_second[0] + (1.0 - BETA_TWO) * grads * grads
    step_size = first_moment / correct_one / (jnp.sqrt(second_moment / correct_two) + ADAM_EPS)
    inner_weights = (
        new_anchor.astype(jnp.float32) * (1.0 - INNER_RATE * DECAY) - INNER_RATE * step_size
    ).astype(jnp.bfloat16)
    return (
        new_anchor,
        new_moment,
        inner_weights[None],
        first_moment[None],
        second_moment[None],
        input_grad,
    )


def physical_mesh(mesh):
    groups = mesh.shape["group"]
    shards = mesh.shape["fsdp"]
    cores = 2
    y_hi = 2
    x = int(round((shards // y_hi) ** 0.5))
    devices = mesh.devices.reshape(groups // cores, cores, y_hi, x, shards // (y_hi * x))
    return Mesh(devices, GROUP + FSDP)


def solution(mesh):
    pmesh = physical_mesh(mesh)
    rows = P(FSDP, None)
    stacked = P(GROUP, FSDP, None)
    tokens = P(GROUP + FSDP, None)
    return jax.shard_map(
        per_device,
        mesh=pmesh,
        in_specs=(rows, stacked, rows, stacked, stacked, tokens, tokens),
        out_specs=(rows, rows, stacked, stacked, stacked, tokens),
        check_vma=False,
    )
```

```python
import jax
import jax.numpy as jnp
from jax import lax
from jax.sharding import Mesh
from jax.sharding import PartitionSpec as P

OUTER_RATE = 0.7
MOMENTUM = 0.9
INNER_RATE = 0.05
BETA_ONE = 0.9
BETA_TWO = 0.95
ADAM_EPS = 1e-08
DECAY = 0.1
ADAM_STEP = 100

GROUP = ("y_lo", "core")
TEAMS = ("y_hi", "x")
TEAM = "z"
FSDP = TEAMS + (TEAM,)


def per_device(anchor, pseudo_grads, outer_moment, adam_first, adam_second, inputs, key_cotangent):
    tok, width = inputs.shape
    rows, kv = anchor.shape
    scale = width ** (-0.5)
    workers = lax.axis_size(GROUP)
    teams = lax.axis_size(TEAMS)
    team = lax.axis_size(TEAM)

    cot_team = lax.all_gather(key_cotangent, TEAM, axis=0, tiled=True)
    hi = lax.axis_size("y_hi")
    cols = inputs.reshape(tok, hi, teams // hi, team, rows).transpose(0, 2, 1, 3, 4)
    inputs_part = lax.all_to_all(
        cols.reshape(tok, teams, team, rows), TEAM, split_axis=2, concat_axis=0, tiled=True
    ).reshape(team * tok, teams * rows)

    own = pseudo_grads[0]
    pair = own.astype(jnp.float32) + lax.ppermute(own, "y_lo", perm=[(0, 1), (1, 0)]).astype(
        jnp.float32
    )
    total = pair + lax.ppermute(pair, "core", perm=[(0, 1), (1, 0)])
    mean_delta = total / workers
    new_moment = MOMENTUM * outer_moment + mean_delta
    new_anchor = (
        anchor.astype(jnp.float32) - OUTER_RATE * (mean_delta + MOMENTUM * new_moment)
    ).astype(jnp.bfloat16)
    new_anchor = lax.optimization_barrier(new_anchor)

    half = kv // 2
    core = lax.axis_index("core")
    mine = lax.all_gather(
        lax.dynamic_slice_in_dim(new_anchor, core * half, half, axis=1), TEAMS, axis=0, tiled=True
    )
    other = lax.ppermute(mine, "core", perm=[(0, 1), (1, 0)])
    cot_mine = lax.dynamic_slice_in_dim(cot_team, core * half, half, axis=1)
    cot_other = lax.dynamic_slice_in_dim(cot_team, (1 - core) * half, half, axis=1)
    product = jnp.einsum(
        "tk,dk->td", cot_mine, mine, preferred_element_type=jnp.float32
    ) + jnp.einsum("tk,dk->td", cot_other, other, preferred_element_type=jnp.float32)
    input_part = (product * scale).astype(jnp.bfloat16)
    input_grad = lax.all_to_all(
        input_part.reshape(team, tok, teams, 1, rows), TEAM, split_axis=0, concat_axis=3, tiled=True
    ).reshape(tok, width)

    partial = (
        jnp.einsum("td,tk->dk", inputs_part, cot_team, preferred_element_type=jnp.float32) * scale
    ).astype(jnp.bfloat16)
    halves = lax.psum_scatter(partial, "x", scatter_dimension=0, tiled=True).reshape(hi, rows, kv)
    y = lax.axis_index("y_hi")
    kept = lax.dynamic_index_in_dim(halves, y, axis=0, keepdims=False)
    given = lax.dynamic_index_in_dim(halves, 1 - y, axis=0, keepdims=False)
    grads = kept.astype(jnp.float32) + lax.ppermute(
        given, "y_hi", perm=[(0, 1), (1, 0)]
    ).astype(jnp.float32)

    correct_one = 1.0 - BETA_ONE**ADAM_STEP
    correct_two = 1.0 - BETA_TWO**ADAM_STEP
    first_moment = BETA_ONE * adam_first[0] + (1.0 - BETA_ONE) * grads
    second_moment = BETA_TWO * adam_second[0] + (1.0 - BETA_TWO) * grads * grads
    step_size = first_moment / correct_one / (jnp.sqrt(second_moment / correct_two) + ADAM_EPS)
    inner_weights = (
        new_anchor.astype(jnp.float32) * (1.0 - INNER_RATE * DECAY) - INNER_RATE * step_size
    ).astype(jnp.bfloat16)
    return (
        new_anchor,
        new_moment,
        inner_weights[None],
        first_moment[None],
        second_moment[None],
        input_grad,
    )


def physical_mesh(mesh):
    groups = mesh.shape["group"]
    shards = mesh.shape["fsdp"]
    cores = 2
    y_hi = 2
    x = int(round((shards // y_hi) ** 0.5))
    devices = mesh.devices.reshape(groups // cores, cores, y_hi, x, shards // (y_hi * x))
    return Mesh(devices, GROUP + FSDP)


def solution(mesh):
    pmesh = physical_mesh(mesh)
    rows = P(FSDP, None)
    stacked = P(GROUP, FSDP, None)
    tokens = P(GROUP + FSDP, None)
    return jax.shard_map(
        per_device,
        mesh=pmesh,
        in_specs=(rows, stacked, rows, stacked, stacked, tokens, tokens),
        out_specs=(rows, rows, stacked, stacked, stacked, tokens),
        check_vma=False,
    )
```

```python
import jax
import jax.numpy as jnp
from jax import lax
from jax.sharding import Mesh
from jax.sharding import PartitionSpec as P

OUTER_RATE = 0.7
MOMENTUM = 0.9
INNER_RATE = 0.05
BETA_ONE = 0.9
BETA_TWO = 0.95
ADAM_EPS = 1e-08
DECAY = 0.1
ADAM_STEP = 100

GROUP = ("y_lo", "core")
TEAMS = ("y_hi", "x")
TEAM = "z"
FSDP = TEAMS + (TEAM,)


def per_device(anchor, pseudo_grads, outer_moment, adam_first, adam_second, inputs, key_cotangent):
    tok, width = inputs.shape
    rows, kv = anchor.shape
    scale = width ** (-0.5)
    workers = lax.axis_size(GROUP)
    teams = lax.axis_size(TEAMS)
    team = lax.axis_size(TEAM)

    cot_team = lax.all_gather(key_cotangent, TEAM, axis=0, tiled=True)
    inputs_part = lax.all_to_all(
        inputs.reshape(tok, teams, team, rows), TEAM, split_axis=2, concat_axis=0, tiled=True
    ).reshape(team * tok, teams * rows)

    own = pseudo_grads[0]
    pair = own.astype(jnp.float32) + lax.ppermute(own, "y_lo", perm=[(0, 1), (1, 0)]).astype(
        jnp.float32
    )
    total = pair + lax.ppermute(pair, "core", perm=[(0, 1), (1, 0)])
    mean_delta = total / workers
    new_moment = MOMENTUM * outer_moment + mean_delta
    new_anchor = (
        anchor.astype(jnp.float32) - OUTER_RATE * (mean_delta + MOMENTUM * new_moment)
    ).astype(jnp.bfloat16)
    new_anchor = lax.optimization_barrier(new_anchor)

    half = kv // 2
    core = lax.axis_index("core")
    mine = lax.all_gather(
        lax.dynamic_slice_in_dim(new_anchor, core * half, half, axis=1), TEAMS, axis=0, tiled=True
    )
    other = lax.ppermute(mine, "core", perm=[(0, 1), (1, 0)])
    cot_mine = lax.dynamic_slice_in_dim(cot_team, core * half, half, axis=1)
    cot_other = lax.dynamic_slice_in_dim(cot_team, (1 - core) * half, half, axis=1)
    product = jnp.einsum(
        "tk,dk->td", cot_mine, mine, preferred_element_type=jnp.float32
    ) + jnp.einsum("tk,dk->td", cot_other, other, preferred_element_type=jnp.float32)
    input_part = (product * scale).astype(jnp.bfloat16)
    input_grad = lax.all_to_all(
        input_part.reshape(team, tok, teams, 1, rows), TEAM, split_axis=0, concat_axis=3, tiled=True
    ).reshape(tok, width)

    partial = (
        jnp.einsum("td,tk->dk", inputs_part, cot_team, preferred_element_type=jnp.float32) * scale
    ).astype(jnp.bfloat16)
    hi = lax.axis_size("y_hi")
    halves = lax.psum_scatter(
        partial.reshape(hi, -1, kv), "x", scatter_dimension=1, tiled=True
    )
    y = lax.axis_index("y_hi")
    kept = lax.dynamic_index_in_dim(halves, y, axis=0, keepdims=False)
    given = lax.dynamic_index_in_dim(halves, 1 - y, axis=0, keepdims=False)
    grads = kept.astype(jnp.float32) + lax.ppermute(
        given, "y_hi", perm=[(0, 1), (1, 0)]
    ).astype(jnp.float32)

    correct_one = 1.0 - BETA_ONE**ADAM_STEP
    correct_two = 1.0 - BETA_TWO**ADAM_STEP
    first_moment = BETA_ONE * adam_first[0] + (1.0 - BETA_ONE) * grads
    second_moment = BETA_TWO * adam_second[0] + (1.0 - BETA_TWO) * grads * grads
    step_size = first_moment / correct_one / (jnp.sqrt(second_moment / correct_two) + ADAM_EPS)
    inner_weights = (
        new_anchor.astype(jnp.float32) * (1.0 - INNER_RATE * DECAY) - INNER_RATE * step_size
    ).astype(jnp.bfloat16)
    return (
        new_anchor,
        new_moment,
        inner_weights[None],
        first_moment[None],
        second_moment[None],
        input_grad,
    )


def physical_mesh(mesh):
    groups = mesh.shape["group"]
    shards = mesh.shape["fsdp"]
    cores = 2
    y_hi = 2
    x = int(round((shards // y_hi) ** 0.5))
    devices = mesh.devices.reshape(groups // cores, cores, y_hi, x, shards // (y_hi * x))
    return Mesh(devices, GROUP + FSDP)


def solution(mesh):
    pmesh = physical_mesh(mesh)
    rows = P(FSDP, None)
    stacked = P(GROUP, FSDP, None)
    tokens = P(GROUP + FSDP, None)
    return jax.shard_map(
        per_device,
        mesh=pmesh,
        in_specs=(rows, stacked, rows, stacked, stacked, tokens, tokens),
        out_specs=(rows, rows, stacked, stacked, stacked, tokens),
        check_vma=False,
    )
```

```python
import jax
import jax.numpy as jnp
from jax import lax
from jax.sharding import Mesh
from jax.sharding import PartitionSpec as P

OUTER_RATE = 0.7
MOMENTUM = 0.9
INNER_RATE = 0.05
BETA_ONE = 0.9
BETA_TWO = 0.95
ADAM_EPS = 1e-08
DECAY = 0.1
ADAM_STEP = 100

GROUP = ("y_lo", "core")
TEAMS = ("y_hi", "x")
TEAM = "z"
FSDP = TEAMS + (TEAM,)


def per_device(anchor, pseudo_grads, outer_moment, adam_first, adam_second, inputs, key_cotangent):
    tok, width = inputs.shape
    rows, kv = anchor.shape
    scale = width ** (-0.5)
    workers = lax.axis_size(GROUP)
    teams = lax.axis_size(TEAMS)
    team = lax.axis_size(TEAM)

    cot_team = lax.all_gather(key_cotangent, TEAM, axis=0, tiled=True)
    inputs_part = lax.all_to_all(
        inputs.reshape(tok, teams, team, rows), TEAM, split_axis=2, concat_axis=0, tiled=True
    ).reshape(team * tok, teams * rows)

    own = pseudo_grads[0]
    pair = own.astype(jnp.float32) + lax.ppermute(own, "y_lo", perm=[(0, 1), (1, 0)]).astype(
        jnp.float32
    )
    total = pair + lax.ppermute(pair, "core", perm=[(0, 1), (1, 0)])
    mean_delta = total / workers
    new_moment = MOMENTUM * outer_moment + mean_delta
    new_anchor = (
        anchor.astype(jnp.float32) - OUTER_RATE * (mean_delta + MOMENTUM * new_moment)
    ).astype(jnp.bfloat16)
    new_anchor = lax.optimization_barrier(new_anchor)

    half = kv // 2
    core = lax.axis_index("core")
    near = lax.all_gather(
        lax.dynamic_slice_in_dim(new_anchor, core * half, half, axis=1), "x", axis=0, tiled=True
    )
    far = lax.ppermute(near, "y_hi", perm=[(0, 1), (1, 0)])
    low = lax.axis_index("y_hi") == 0
    mine = jnp.concatenate([jnp.where(low, near, far), jnp.where(low, far, near)], axis=0)
    other = lax.ppermute(mine, "core", perm=[(0, 1), (1, 0)])
    cot_mine = lax.dynamic_slice_in_dim(cot_team, core * half, half, axis=1)
    cot_other = lax.dynamic_slice_in_dim(cot_team, (1 - core) * half, half, axis=1)
    product = jnp.einsum(
        "tk,dk->td", cot_mine, mine, preferred_element_type=jnp.float32
    ) + jnp.einsum("tk,dk->td", cot_other, other, preferred_element_type=jnp.float32)
    input_part = (product * scale).astype(jnp.bfloat16)
    input_grad = lax.all_to_all(
        input_part.reshape(team, tok, teams, 1, rows), TEAM, split_axis=0, concat_axis=3, tiled=True
    ).reshape(tok, width)

    partial = (
        jnp.einsum("td,tk->dk", inputs_part, cot_team, preferred_element_type=jnp.float32) * scale
    ).astype(jnp.bfloat16)
    hi = lax.axis_size("y_hi")
    halves = lax.psum_scatter(
        partial.reshape(hi, -1, kv), "x", scatter_dimension=1, tiled=True
    )
    y = lax.axis_index("y_hi")
    kept = lax.dynamic_index_in_dim(halves, y, axis=0, keepdims=False)
    given = lax.dynamic_index_in_dim(halves, 1 - y, axis=0, keepdims=False)
    grads = kept.astype(jnp.float32) + lax.ppermute(
        given, "y_hi", perm=[(0, 1), (1, 0)]
    ).astype(jnp.float32)

    correct_one = 1.0 - BETA_ONE**ADAM_STEP
    correct_two = 1.0 - BETA_TWO**ADAM_STEP
    first_moment = BETA_ONE * adam_first[0] + (1.0 - BETA_ONE) * grads
    second_moment = BETA_TWO * adam_second[0] + (1.0 - BETA_TWO) * grads * grads
    step_size = first_moment / correct_one / (jnp.sqrt(second_moment / correct_two) + ADAM_EPS)
    inner_weights = (
        new_anchor.astype(jnp.float32) * (1.0 - INNER_RATE * DECAY) - INNER_RATE * step_size
    ).astype(jnp.bfloat16)
    return (
        new_anchor,
        new_moment,
        inner_weights[None],
        first_moment[None],
        second_moment[None],
        input_grad,
    )


def physical_mesh(mesh):
    groups = mesh.shape["group"]
    shards = mesh.shape["fsdp"]
    cores = 2
    y_hi = 2
    x = int(round((shards // y_hi) ** 0.5))
    devices = mesh.devices.reshape(groups // cores, cores, y_hi, x, shards // (y_hi * x))
    return Mesh(devices, GROUP + FSDP)


def solution(mesh):
    pmesh = physical_mesh(mesh)
    rows = P(FSDP, None)
    stacked = P(GROUP, FSDP, None)
    tokens = P(GROUP + FSDP, None)
    return jax.shard_map(
        per_device,
        mesh=pmesh,
        in_specs=(rows, stacked, rows, stacked, stacked, tokens, tokens),
        out_specs=(rows, rows, stacked, stacked, stacked, tokens),
        check_vma=False,
    )
```

```python
import jax
import jax.numpy as jnp
from jax import lax
from jax.sharding import Mesh
from jax.sharding import PartitionSpec as P

OUTER_RATE = 0.7
MOMENTUM = 0.9
INNER_RATE = 0.05
BETA_ONE = 0.9
BETA_TWO = 0.95
ADAM_EPS = 1e-08
DECAY = 0.1
ADAM_STEP = 100

GROUP = ("y_lo", "core")
TEAMS = ("y_hi", "x")
TEAM = "z"
FSDP = TEAMS + (TEAM,)


def per_device(anchor, pseudo_grads, outer_moment, adam_first, adam_second, inputs, key_cotangent):
    tok, width = inputs.shape
    rows, kv = anchor.shape
    scale = width ** (-0.5)
    workers = lax.axis_size(GROUP)
    teams = lax.axis_size(TEAMS)
    team = lax.axis_size(TEAM)

    cot_team = lax.all_gather(key_cotangent, TEAM, axis=0, tiled=True)

    own = pseudo_grads[0]
    cols = inputs.reshape(tok, teams, team, rows).transpose(2, 1, 0, 3)
    got, cols = lax.optimization_barrier((lax.ppermute(own, "y_lo", perm=[(0, 1), (1, 0)]), cols))
    pair = own.astype(jnp.float32) + got.astype(jnp.float32)
    total = pair + lax.ppermute(pair, "core", perm=[(0, 1), (1, 0)])
    mean_delta = total / workers
    inputs_part = (
        lax.all_to_all(cols, TEAM, split_axis=0, concat_axis=0, tiled=True)
        .transpose(0, 2, 1, 3)
        .reshape(team * tok, teams * rows)
    )
    new_moment = MOMENTUM * outer_moment + mean_delta
    new_anchor = (
        anchor.astype(jnp.float32) - OUTER_RATE * (mean_delta + MOMENTUM * new_moment)
    ).astype(jnp.bfloat16)
    new_anchor = lax.optimization_barrier(new_anchor)

    half = kv // 2
    core = lax.axis_index("core")
    mine = lax.all_gather(
        lax.dynamic_slice_in_dim(new_anchor, core * half, half, axis=1), TEAMS, axis=0, tiled=True
    )
    other = lax.ppermute(mine, "core", perm=[(0, 1), (1, 0)])
    cot_mine = lax.dynamic_slice_in_dim(cot_team, core * half, half, axis=1)
    cot_other = lax.dynamic_slice_in_dim(cot_team, (1 - core) * half, half, axis=1)
    product = jnp.einsum(
        "tk,dk->td", cot_mine, mine, preferred_element_type=jnp.float32
    ) + jnp.einsum("tk,dk->td", cot_other, other, preferred_element_type=jnp.float32)
    input_part = (product * scale).astype(jnp.bfloat16)
    input_grad = lax.all_to_all(
        input_part.reshape(team, tok, teams, 1, rows), TEAM, split_axis=0, concat_axis=3, tiled=True
    ).reshape(tok, width)

    partial = (
        jnp.einsum("td,tk->dk", inputs_part, cot_team, preferred_element_type=jnp.float32) * scale
    ).astype(jnp.bfloat16)
    hi = lax.axis_size("y_hi")
    halves = lax.psum_scatter(
        partial.reshape(hi, -1, kv), "x", scatter_dimension=1, tiled=True
    )
    y = lax.axis_index("y_hi")
    kept = lax.dynamic_index_in_dim(halves, y, axis=0, keepdims=False)
    given = lax.dynamic_index_in_dim(halves, 1 - y, axis=0, keepdims=False)
    grads = kept.astype(jnp.float32) + lax.ppermute(
        given, "y_hi", perm=[(0, 1), (1, 0)]
    ).astype(jnp.float32)

    correct_one = 1.0 - BETA_ONE**ADAM_STEP
    correct_two = 1.0 - BETA_TWO**ADAM_STEP
    first_moment = BETA_ONE * adam_first[0] + (1.0 - BETA_ONE) * grads
    second_moment = BETA_TWO * adam_second[0] + (1.0 - BETA_TWO) * grads * grads
    step_size = first_moment / correct_one / (jnp.sqrt(second_moment / correct_two) + ADAM_EPS)
    inner_weights = (
        new_anchor.astype(jnp.float32) * (1.0 - INNER_RATE * DECAY) - INNER_RATE * step_size
    ).astype(jnp.bfloat16)
    return (
        new_anchor,
        new_moment,
        inner_weights[None],
        first_moment[None],
        second_moment[None],
        input_grad,
    )


def physical_mesh(mesh):
    groups = mesh.shape["group"]
    shards = mesh.shape["fsdp"]
    cores = 2
    y_hi = 2
    x = int(round((shards // y_hi) ** 0.5))
    devices = mesh.devices.reshape(groups // cores, cores, y_hi, x, shards // (y_hi * x))
    return Mesh(devices, GROUP + FSDP)


def solution(mesh):
    pmesh = physical_mesh(mesh)
    rows = P(FSDP, None)
    stacked = P(GROUP, FSDP, None)
    tokens = P(GROUP + FSDP, None)
    return jax.shard_map(
        per_device,
        mesh=pmesh,
        in_specs=(rows, stacked, rows, stacked, stacked, tokens, tokens),
        out_specs=(rows, rows, stacked, stacked, stacked, tokens),
        check_vma=False,
    )
```

```python
import jax
import jax.numpy as jnp
from jax import lax
from jax.sharding import Mesh
from jax.sharding import PartitionSpec as P

OUTER_RATE = 0.7
MOMENTUM = 0.9
INNER_RATE = 0.05
BETA_ONE = 0.9
BETA_TWO = 0.95
ADAM_EPS = 1e-08
DECAY = 0.1
ADAM_STEP = 100

GROUP = ("y_lo", "core")
TEAMS = ("y_hi", "x")
TEAM = "z"
FSDP = TEAMS + (TEAM,)


def per_device(anchor, pseudo_grads, outer_moment, adam_first, adam_second, inputs, key_cotangent):
    tok, width = inputs.shape
    rows, kv = anchor.shape
    scale = width ** (-0.5)
    workers = lax.axis_size(GROUP)
    teams = lax.axis_size(TEAMS)
    team = lax.axis_size(TEAM)

    cot_team = lax.all_gather(key_cotangent, TEAM, axis=0, tiled=True)
    inputs_part = lax.all_to_all(
        inputs.reshape(tok, teams, team, rows), TEAM, split_axis=2, concat_axis=0, tiled=True
    ).reshape(team * tok, teams * rows)

    own = pseudo_grads[0]
    pair = own.astype(jnp.float32) + lax.ppermute(own, "y_lo", perm=[(0, 1), (1, 0)]).astype(
        jnp.float32
    )
    total = pair + lax.ppermute(pair, "core", perm=[(0, 1), (1, 0)])
    mean_delta = total / workers
    new_moment = MOMENTUM * outer_moment + mean_delta
    new_anchor = (
        anchor.astype(jnp.float32) - OUTER_RATE * (mean_delta + MOMENTUM * new_moment)
    ).astype(jnp.bfloat16)
    new_anchor = lax.optimization_barrier(new_anchor)

    half = kv // 2
    core = lax.axis_index("core")
    mine = lax.all_gather(
        lax.dynamic_slice_in_dim(new_anchor, core * half, half, axis=1), TEAMS, axis=0, tiled=True
    )
    other = lax.ppermute(mine, "core", perm=[(0, 1), (1, 0)])
    cot_mine = lax.dynamic_slice_in_dim(cot_team, core * half, half, axis=1)
    cot_other = lax.dynamic_slice_in_dim(cot_team, (1 - core) * half, half, axis=1)
    pieces = []
    for h in range(2):
        rows_h = slice(h * (teams // 2) * rows, (h + 1) * (teams // 2) * rows)
        product = jnp.einsum(
            "tk,dk->td", cot_mine, mine[rows_h], preferred_element_type=jnp.float32
        ) + jnp.einsum("tk,dk->td", cot_other, other[rows_h], preferred_element_type=jnp.float32)
        input_part = (product * scale).astype(jnp.bfloat16)
        pieces.append(
            lax.all_to_all(
                input_part.reshape(team, tok, teams // 2, 1, rows),
                TEAM,
                split_axis=0,
                concat_axis=3,
                tiled=True,
            ).reshape(tok, width // 2)
        )
    input_grad = jnp.concatenate(pieces, axis=1)

    partial = (
        jnp.einsum("td,tk->dk", inputs_part, cot_team, preferred_element_type=jnp.float32) * scale
    ).astype(jnp.bfloat16)
    hi = lax.axis_size("y_hi")
    halves = lax.psum_scatter(
        partial.reshape(hi, -1, kv), "x", scatter_dimension=1, tiled=True
    )
    y = lax.axis_index("y_hi")
    kept = lax.dynamic_index_in_dim(halves, y, axis=0, keepdims=False)
    given = lax.dynamic_index_in_dim(halves, 1 - y, axis=0, keepdims=False)
    grads = kept.astype(jnp.float32) + lax.ppermute(
        given, "y_hi", perm=[(0, 1), (1, 0)]
    ).astype(jnp.float32)

    correct_one = 1.0 - BETA_ONE**ADAM_STEP
    correct_two = 1.0 - BETA_TWO**ADAM_STEP
    first_moment = BETA_ONE * adam_first[0] + (1.0 - BETA_ONE) * grads
    second_moment = BETA_TWO * adam_second[0] + (1.0 - BETA_TWO) * grads * grads
    step_size = first_moment / correct_one / (jnp.sqrt(second_moment / correct_two) + ADAM_EPS)
    inner_weights = (
        new_anchor.astype(jnp.float32) * (1.0 - INNER_RATE * DECAY) - INNER_RATE * step_size
    ).astype(jnp.bfloat16)
    return (
        new_anchor,
        new_moment,
        inner_weights[None],
        first_moment[None],
        second_moment[None],
        input_grad,
    )


def physical_mesh(mesh):
    groups = mesh.shape["group"]
    shards = mesh.shape["fsdp"]
    cores = 2
    y_hi = 2
    x = int(round((shards // y_hi) ** 0.5))
    devices = mesh.devices.reshape(groups // cores, cores, y_hi, x, shards // (y_hi * x))
    return Mesh(devices, GROUP + FSDP)


def solution(mesh):
    pmesh = physical_mesh(mesh)
    rows = P(FSDP, None)
    stacked = P(GROUP, FSDP, None)
    tokens = P(GROUP + FSDP, None)
    return jax.shard_map(
        per_device,
        mesh=pmesh,
        in_specs=(rows, stacked, rows, stacked, stacked, tokens, tokens),
        out_specs=(rows, rows, stacked, stacked, stacked, tokens),
        check_vma=False,
    )
```

```python
import jax
import jax.numpy as jnp
from jax import lax
from jax.sharding import Mesh
from jax.sharding import PartitionSpec as P

OUTER_RATE = 0.7
MOMENTUM = 0.9
INNER_RATE = 0.05
BETA_ONE = 0.9
BETA_TWO = 0.95
ADAM_EPS = 1e-08
DECAY = 0.1
ADAM_STEP = 100

GROUP = ("y_lo", "core")
TEAMS = ("y_hi", "x")
TEAM = "z"
FSDP = TEAMS + (TEAM,)


def per_device(anchor, pseudo_grads, outer_moment, adam_first, adam_second, inputs, key_cotangent):
    tok, width = inputs.shape
    rows, kv = anchor.shape
    scale = width ** (-0.5)
    workers = lax.axis_size(GROUP)
    teams = lax.axis_size(TEAMS)
    team = lax.axis_size(TEAM)

    cot_team = lax.all_gather(key_cotangent, TEAM, axis=0, tiled=True)
    inputs_part = lax.all_to_all(
        inputs.reshape(tok, teams, team, rows), TEAM, split_axis=2, concat_axis=0, tiled=True
    ).reshape(team * tok, teams * rows)

    own = pseudo_grads[0]
    core = lax.axis_index("core")
    pair = own.astype(jnp.float32) + lax.ppermute(own, "core", perm=[(0, 1), (1, 0)]).astype(
        jnp.float32
    )
    share = lax.dynamic_slice_in_dim(pair, core * (rows // 2), rows // 2, axis=0).astype(
        jnp.bfloat16
    )
    done = share.astype(jnp.float32) + lax.ppermute(
        share, "y_lo", perm=[(0, 1), (1, 0)]
    ).astype(jnp.float32)
    rest = lax.ppermute(done, "core", perm=[(0, 1), (1, 0)])
    low = core == 0
    total = jnp.concatenate([jnp.where(low, done, rest), jnp.where(low, rest, done)], axis=0)
    mean_delta = total / workers
    new_moment = MOMENTUM * outer_moment + mean_delta
    new_anchor = (
        anchor.astype(jnp.float32) - OUTER_RATE * (mean_delta + MOMENTUM * new_moment)
    ).astype(jnp.bfloat16)
    new_anchor = lax.optimization_barrier(new_anchor)

    half = kv // 2
    core = lax.axis_index("core")
    mine = lax.all_gather(
        lax.dynamic_slice_in_dim(new_anchor, core * half, half, axis=1), TEAMS, axis=0, tiled=True
    )
    other = lax.ppermute(mine, "core", perm=[(0, 1), (1, 0)])
    cot_mine = lax.dynamic_slice_in_dim(cot_team, core * half, half, axis=1)
    cot_other = lax.dynamic_slice_in_dim(cot_team, (1 - core) * half, half, axis=1)
    product = jnp.einsum(
        "tk,dk->td", cot_mine, mine, preferred_element_type=jnp.float32
    ) + jnp.einsum("tk,dk->td", cot_other, other, preferred_element_type=jnp.float32)
    input_part = (product * scale).astype(jnp.bfloat16)
    input_grad = lax.all_to_all(
        input_part.reshape(team, tok, teams, 1, rows), TEAM, split_axis=0, concat_axis=3, tiled=True
    ).reshape(tok, width)

    partial = (
        jnp.einsum("td,tk->dk", inputs_part, cot_team, preferred_element_type=jnp.float32) * scale
    ).astype(jnp.bfloat16)
    hi = lax.axis_size("y_hi")
    halves = lax.psum_scatter(
        partial.reshape(hi, -1, kv), "x", scatter_dimension=1, tiled=True
    )
    y = lax.axis_index("y_hi")
    kept = lax.dynamic_index_in_dim(halves, y, axis=0, keepdims=False)
    given = lax.dynamic_index_in_dim(halves, 1 - y, axis=0, keepdims=False)
    grads = kept.astype(jnp.float32) + lax.ppermute(
        given, "y_hi", perm=[(0, 1), (1, 0)]
    ).astype(jnp.float32)

    correct_one = 1.0 - BETA_ONE**ADAM_STEP
    correct_two = 1.0 - BETA_TWO**ADAM_STEP
    first_moment = BETA_ONE * adam_first[0] + (1.0 - BETA_ONE) * grads
    second_moment = BETA_TWO * adam_second[0] + (1.0 - BETA_TWO) * grads * grads
    step_size = first_moment / correct_one / (jnp.sqrt(second_moment / correct_two) + ADAM_EPS)
    inner_weights = (
        new_anchor.astype(jnp.float32) * (1.0 - INNER_RATE * DECAY) - INNER_RATE * step_size
    ).astype(jnp.bfloat16)
    return (
        new_anchor,
        new_moment,
        inner_weights[None],
        first_moment[None],
        second_moment[None],
        input_grad,
    )


def physical_mesh(mesh):
    groups = mesh.shape["group"]
    shards = mesh.shape["fsdp"]
    cores = 2
    y_hi = 2
    x = int(round((shards // y_hi) ** 0.5))
    devices = mesh.devices.reshape(groups // cores, cores, y_hi, x, shards // (y_hi * x))
    return Mesh(devices, GROUP + FSDP)


def solution(mesh):
    pmesh = physical_mesh(mesh)
    rows = P(FSDP, None)
    stacked = P(GROUP, FSDP, None)
    tokens = P(GROUP + FSDP, None)
    return jax.shard_map(
        per_device,
        mesh=pmesh,
        in_specs=(rows, stacked, rows, stacked, stacked, tokens, tokens),
        out_specs=(rows, rows, stacked, stacked, stacked, tokens),
        check_vma=False,
    )
```
